512 devices in a mesh: series: 8 (over y_hi, x), tm: 64 (over z, y_lo, core).
Axes of the slice: x: 4, y: 8 (y_hi: 2, y_lo: 4; y = y_hi * 4 + y_lo), z: 8, core: 2. Of those that a mesh axis runs over, the one named last changes fastest.
Arguments:
- y_obs: bfloat16 [32768, 32768], P('series', 'tm'), may hold values from -6 to 6
- tile_mask: int32 [256, 256], P('series', 'tm'), may hold values 0 or 1
- factors: float32 [32768, 128], P(('series', 'tm')), may hold values from -0.5 to 0.5
- adam_m: float32 [32768, 128], P(('series', 'tm')), may hold values from -3 to 3
- adam_v: float32 [32768, 128], P(('series', 'tm')), may hold values from 0.1 to 10
- basis: float32 [128, 32768], P('series', 'tm'), may hold values from -6 to 6
- dilations: int32 [4], replicated, may hold values from 1 to 32, as said below
- conv_w: bfloat16 [4, 2, 128, 128], replicated, may hold values from -0.375 to 0.375
- conv_b: float32 [4, 128], replicated, may hold values from -3 to 3
Outputs:
- factors_new: float32 [32768, 128], P(('series', 'tm'))
- m_new: float32 [32768, 128], P(('series', 'tm'))
- v_new: float32 [32768, 128], P(('series', 'tm'))
- basis_new: float32 [128, 32768], P('series', 'tm')
The draws below stay inside these ranges and needn't reach their ends.
Inputs may be any that keep to these rules, and one draw needn't show every extreme that they name: `dilations`: at least one layer has dilation 32.
All inputs are finite; a program needn't handle non-finite values. No bound on the sum of `tile_mask` on one device may be relied on, other than what follows from the above.
Results may differ from the reference program's by a relative error of at most 0.0031.
Values may be sent and summed in bfloat16 or wider, within the bound.
No kernel may reach another device: no remote copies, remote signals or barrier semaphores. Data moves between devices by JAX's collectives and lax.ppermute only.
A program may use at most 64 MiB of HBM per device.

```python
import math
import jax
import jax.numpy as jnp
from jax import lax

K = 128
TILE = 128
LAYERS = 4
D_MAX = 32
NS = 32768
NT = 32768


def draw_dilations(key, part):
    first, second = jax.random.split(jax.random.fold_in(key, 17))
    values = jax.random.randint(first, (LAYERS,), 1, D_MAX + 1).astype(jnp.int32)
    where_top = jax.random.randint(second, (), 0, LAYERS)
    return values.at[where_top].set(D_MAX).astype(jnp.int32)


def set_ends(entries, key, smallest, top_value):
    dims = entries.shape
    place = [jax.random.randint(jax.random.fold_in(key, axis), (), 0, dims[axis]) for axis in range(len(dims))]
    entries = entries.at[tuple(place)].set(smallest)
    longest = dims.index(max(dims))
    place[longest] = (place[longest] + 1) % dims[longest]
    return entries.at[tuple(place)].set(top_value)


def steps_of(key, dims, cuts, least, top_value):
    def one(position, shards_of):
        steps = jax.random.uniform(jax.random.fold_in(jax.random.fold_in(key, 6), position), (shards_of,), jnp.float32, least / len(cuts), top_value / len(cuts))
        return jnp.repeat(jnp.exp(steps), dims[position] // shards_of).reshape((-1,) + (1,) * (len(dims) - position - 1))

    level = one(*cuts[0])
    for cut in cuts[1:]:
        level = level * one(*cut)
    return level


def noise(rng, extent, scale, reach, cuts=(), dtype=jnp.bfloat16):
    values = scale * jax.random.normal(rng, extent, jnp.float32)
    if cuts:
        values = values * steps_of(rng, extent, cuts, -0.22, 0.18)
    return jnp.clip(values, -reach, reach).astype(dtype)


def setup_inputs(seed: int = 0) -> dict:
    streams_of = jax.random.split(jax.random.key(seed), 10)
    y_obs = noise(streams_of[0], (NS, NT), 1.0, 6.0, ((0, 8), (1, 64)))
    tile_mask = set_ends((jax.random.randint(streams_of[1], (NS // TILE, NT // TILE), 0, 4) < 3).astype(jnp.int32), jax.random.fold_in(streams_of[1], 1), 0, 1)
    factors = noise(streams_of[2], (NS, K), K ** -0.5, 0.5, ((0, 512),), jnp.float32)
    adam_m = noise(streams_of[3], (NS, K), 0.5, 3.0, ((0, 512),), jnp.float32)
    adam_v = jnp.clip(jnp.exp(math.log(10.0) - 4.6051702 * jax.random.uniform(streams_of[4], (NS, K), jnp.float32) ** steps_of(streams_of[4], (NS, K), ((0, 512),), -0.2, 0.2)), 0.1, 10.0)
    basis = noise(streams_of[5], (K, NT), 1.0, 6.0, ((0, 8), (1, 64)), jnp.float32)
    dilations = draw_dilations(jax.random.fold_in(streams_of[9], 71), 0)
    conv_w = noise(streams_of[7], (LAYERS, 2, K, K), (2 * K) ** -0.5, 0.375)
    conv_b = noise(streams_of[8], (LAYERS, K), 0.5, 3.0, (), jnp.float32)
    return dict(y_obs=y_obs, tile_mask=tile_mask, factors=factors, adam_m=adam_m, adam_v=adam_v, basis=basis, dilations=dilations, conv_w=conv_w, conv_b=conv_b)


def expand(tiles, tile):
    rows, cols = tiles.shape
    ones = tiles.astype(jnp.float32)
    return jnp.broadcast_to(ones[:, None, :, None], (rows, tile, cols, tile)).reshape(rows * tile, cols * tile)

def adam_update(factors, adam_m, adam_v, grad_f):
    m_new = 0.9 * adam_m + 0.1 * grad_f
    v_new = 0.999 * adam_v + 0.001 * grad_f * grad_f
    m_hat = m_new / (1.0 - 0.9 ** 10)
    v_hat = v_new / (1.0 - 0.999 ** 10)
    return (factors - 0.01 * m_hat / (jnp.sqrt(v_hat) + 1e-08), m_new, v_new)

def reference(y_obs, tile_mask, factors, adam_m, adam_v, basis, dilations, conv_w, conv_b):
    xb = basis.astype(jnp.bfloat16)
    block = math.gcd(NS, 1024)
    count = NS // block
    y_blocks = y_obs.reshape(count, block, NT)
    m_blocks = tile_mask.reshape(count, block // TILE, NT // TILE)
    f_blocks = factors.astype(jnp.bfloat16).reshape(count, block, K)
    scale_f = 1.0 / math.sqrt(NT)

    def sweep(total, item):
        y_part, m_part, f_part = item
        pred = jnp.dot(f_part, xb, preferred_element_type=jnp.float32)
        resid = expand(m_part, TILE) * (y_part.astype(jnp.float32) - pred)
        rb = resid.astype(jnp.bfloat16)
        grad_part = -lax.dot_general(rb, xb, (((1,), (1,)), ((), ())), preferred_element_type=jnp.float32) * scale_f
        total = total - lax.dot_general(f_part, rb, (((0,), (0,)), ((), ())), preferred_element_type=jnp.float32)
        return (total, grad_part)
    total, grads = lax.scan(sweep, jnp.zeros((K, NT), jnp.float32), (y_blocks, m_blocks, f_blocks))
    grad_f = grads.reshape(NS, K)
    grad_x = total * math.sqrt(K / NS)
    factors_new, m_new, v_new = adam_update(factors, adam_m, adam_v, grad_f)
    hidden = xb.astype(jnp.float32)
    for layer in range(LAYERS):
        hb = hidden.astype(jnp.bfloat16)
        padded = jnp.concatenate([jnp.zeros((K, D_MAX), jnp.bfloat16), hb], axis=1)
        past = lax.dynamic_slice_in_dim(padded, (D_MAX - dilations[layer]).astype(jnp.int32), NT, 1)
        z_val = jnp.dot(conv_w[layer, 0], past, preferred_element_type=jnp.float32)
        z_val = z_val + jnp.dot(conv_w[layer, 1], hb, preferred_element_type=jnp.float32)
        z_val = z_val + conv_b[layer][:, None]
        hidden = hidden + jax.nn.relu(z_val)
    basis_new = basis - 0.5 * (grad_x + (basis - hidden))
    return (factors_new, m_new, v_new, basis_new)
```

```python
import math

import jax
import jax.numpy as jnp
from jax import lax
from jax.sharding import Mesh
from jax.sharding import PartitionSpec as P

K = 128
TILE = 128
LAYERS = 4
D_MAX = 32
HALO = LAYERS * D_MAX
CORES = 2
Y_LO = 4
TM = ("z", "ylo", "core")
ROW = ("z", "ylo")


def expand(tiles, tile):
    rows, cols = tiles.shape
    ones = tiles.astype(jnp.float32)
    return jnp.broadcast_to(ones[:, None, :, None], (rows, tile, cols, tile)).reshape(
        rows * tile, cols * tile
    )


def adam_update(factors, adam_m, adam_v, grad_f):
    m_new = 0.9 * adam_m + 0.1 * grad_f
    v_new = 0.999 * adam_v + 0.001 * grad_f * grad_f
    m_hat = m_new / (1.0 - 0.9**10)
    v_hat = v_new / (1.0 - 0.999**10)
    return (factors - 0.01 * m_hat / (jnp.sqrt(v_hat) + 1e-08), m_new, v_new)


def conv_layer(hidden, hb, past, weights, biases):
    z_val = jnp.dot(weights[0], past, preferred_element_type=jnp.float32)
    z_val = z_val + jnp.dot(weights[1], hb, preferred_element_type=jnp.float32)
    z_val = z_val + biases[:, None]
    return hidden + jax.nn.relu(z_val)


def gather_by_a2a(x, axis, count):
    copies = jnp.broadcast_to(x[None], (count,) + x.shape)
    return lax.all_to_all(copies, axis, 0, 0, tiled=True)


def on_device(y_obs, tile_mask, factors, adam_m, adam_v, basis, dilations, conv_w, conv_b):
    own_rows = factors.shape[0]
    width = basis.shape[1]
    rank_part = basis.shape[0]
    n_row = lax.axis_size(ROW)
    n_series = lax.axis_size("series")
    n_tm = n_row * CORES
    total_time = width * n_tm
    total_series = own_rows * n_tm * n_series

    fb = factors.astype(jnp.bfloat16)
    f_rows = gather_by_a2a(fb, ROW, n_row)
    f_all = gather_by_a2a(f_rows, "core", CORES)
    f_block = jnp.swapaxes(f_all, 0, 1).reshape(n_tm * own_rows, K)

    x_parts = gather_by_a2a(basis.astype(jnp.bfloat16), "series", n_series)
    x_full = x_parts.reshape(n_series * rank_part, width)

    pred = jnp.dot(f_block, x_full, preferred_element_type=jnp.float32)
    resid = expand(tile_mask, TILE) * (y_obs.astype(jnp.float32) - pred)
    rb = resid.astype(jnp.bfloat16)
    scale_f = 1.0 / math.sqrt(total_time)
    contract_time = (((1,), (1,)), ((), ()))
    partial_f = -lax.dot_general(rb, x_full, contract_time, preferred_element_type=jnp.float32) * scale_f
    by_core = partial_f.reshape(n_row, CORES, own_rows, K)
    by_core = lax.all_to_all(by_core, "core", 1, 1, tiled=True).sum(1)
    by_row = lax.all_to_all(by_core.astype(jnp.bfloat16), ROW, 0, 0, tiled=True)
    grad_f = by_row.astype(jnp.float32).sum(0)
    factors_new, m_new, v_new = adam_update(factors, adam_m, adam_v, grad_f)

    partial_x = -lax.dot_general(
        f_block, rb, (((0,), (0,)), ((), ())), preferred_element_type=jnp.float32
    )
    partial_x = partial_x * math.sqrt(K / total_series)
    pieces = partial_x.reshape(n_series, rank_part, width)
    grad_x = lax.all_to_all(pieces, "series", 0, 0, tiled=True).sum(0)

    xb = x_full
    halo = lax.ppermute(xb[:, width - HALO :], TM, [(i, i + 1) for i in range(n_tm - 1)])
    first = lax.axis_index(TM) == 0
    column = lax.broadcasted_iota(jnp.int32, (1, HALO + width), 1)
    keep = jnp.logical_or(jnp.logical_not(first), column >= HALO)
    hidden = jnp.concatenate([halo, xb], axis=1).astype(jnp.float32)
    for layer in range(LAYERS):
        hb = jnp.where(keep, hidden, 0.0).astype(jnp.bfloat16)
        extended = jnp.concatenate([jnp.zeros((K, D_MAX), jnp.bfloat16), hb], axis=1)
        past = lax.dynamic_slice_in_dim(extended, D_MAX - dilations[layer], HALO + width, 1)
        hidden = conv_layer(hidden, hb, past, conv_w[layer], conv_b[layer])
    target = lax.dynamic_slice_in_dim(hidden[:, HALO:], lax.axis_index("series") * rank_part, rank_part, 0)
    basis_new = basis - 0.5 * (grad_x + (basis - target))
    return (factors_new, m_new, v_new, basis_new)


def solution(mesh):
    n_series, n_tm = mesh.devices.shape
    devices = mesh.devices.reshape(n_series, n_tm // (Y_LO * CORES), Y_LO, CORES)
    fine = Mesh(devices, ("series",) + TM)
    block = P("series", TM)
    rows = P(("series",) + TM, None)
    return jax.shard_map(
        on_device,
        mesh=fine,
        in_specs=(block, block, rows, rows, rows, block, P(), P(), P()),
        out_specs=(rows, rows, rows, block),
        check_vma=False,
    )
```

```python
import math

import jax
import jax.numpy as jnp
from jax import lax
from jax.sharding import Mesh
from jax.sharding import PartitionSpec as P

K = 128
TILE = 128
LAYERS = 4
D_MAX = 32
HALO = LAYERS * D_MAX
CORES = 2
Y_LO = 4
TM = ("z", "ylo", "core")
ROW = ("z", "ylo")


def expand(tiles, tile):
    rows, cols = tiles.shape
    ones = tiles.astype(jnp.float32)
    return jnp.broadcast_to(ones[:, None, :, None], (rows, tile, cols, tile)).reshape(
        rows * tile, cols * tile
    )


def adam_update(factors, adam_m, adam_v, grad_f):
    m_new = 0.9 * adam_m + 0.1 * grad_f
    v_new = 0.999 * adam_v + 0.001 * grad_f * grad_f
    m_hat = m_new / (1.0 - 0.9**10)
    v_hat = v_new / (1.0 - 0.999**10)
    return (factors - 0.01 * m_hat / (jnp.sqrt(v_hat) + 1e-08), m_new, v_new)


def conv_layer(hidden, hb, past, weights, biases):
    z_val = jnp.dot(weights[0], past, preferred_element_type=jnp.float32)
    z_val = z_val + jnp.dot(weights[1], hb, preferred_element_type=jnp.float32)
    z_val = z_val + biases[:, None]
    return hidden + jax.nn.relu(z_val)


def gather_by_a2a(x, axis, count):
    copies = jnp.broadcast_to(x[None], (count,) + x.shape)
    return lax.all_to_all(copies, axis, 0, 0, tiled=True)


def gather_by_permutes(x, me, count):
    arrived = [x] + [
        lax.ppermute(x, "series", [(i, (i + k) % count) for i in range(count)])
        for k in range(1, count)
    ]
    from_ahead = jnp.stack([arrived[(count - m) % count] for m in range(count)])
    return jnp.roll(from_ahead, me, axis=0)


def reduce_by_permutes(pieces, me, count):
    total = lax.dynamic_index_in_dim(pieces, me, 0, keepdims=False)
    for k in range(1, count):
        piece = lax.dynamic_index_in_dim(pieces, (me + k) % count, 0, keepdims=False)
        total = total + lax.ppermute(piece, "series", [(i, (i + k) % count) for i in range(count)])
    return total


def on_device(y_obs, tile_mask, factors, adam_m, adam_v, basis, dilations, conv_w, conv_b):
    own_rows = factors.shape[0]
    width = basis.shape[1]
    rank_part = basis.shape[0]
    n_row = lax.axis_size(ROW)
    n_series = lax.axis_size("series")
    n_tm = n_row * CORES
    total_time = width * n_tm
    total_series = own_rows * n_tm * n_series

    fb = factors.astype(jnp.bfloat16)
    f_rows = gather_by_a2a(fb, ROW, n_row)
    f_all = gather_by_a2a(f_rows, "core", CORES)
    f_block = jnp.swapaxes(f_all, 0, 1).reshape(n_tm * own_rows, K)

    me = lax.axis_index("series")
    x_parts = gather_by_permutes(basis.astype(jnp.bfloat16), me, n_series)
    x_full = x_parts.reshape(n_series * rank_part, width)

    pred = jnp.dot(f_block, x_full, preferred_element_type=jnp.float32)
    resid = expand(tile_mask, TILE) * (y_obs.astype(jnp.float32) - pred)
    rb = resid.astype(jnp.bfloat16)
    scale_f = 1.0 / math.sqrt(total_time)
    contract_time = (((1,), (1,)), ((), ()))
    partial_f = -lax.dot_general(rb, x_full, contract_time, preferred_element_type=jnp.float32) * scale_f
    by_core = partial_f.reshape(n_row, CORES, own_rows, K)
    by_core = lax.all_to_all(by_core, "core", 1, 1, tiled=True).sum(1)
    by_row = lax.all_to_all(by_core.astype(jnp.bfloat16), ROW, 0, 0, tiled=True)
    grad_f = by_row.astype(jnp.float32).sum(0)
    factors_new, m_new, v_new = adam_update(factors, adam_m, adam_v, grad_f)

    partial_x = -lax.dot_general(
        f_block, rb, (((0,), (0,)), ((), ())), preferred_element_type=jnp.float32
    )
    partial_x = partial_x * math.sqrt(K / total_series)
    pieces = partial_x.reshape(n_series, rank_part, width)
    grad_x = reduce_by_permutes(pieces, me, n_series)

    xb = x_full
    halo = lax.ppermute(xb[:, width - HALO :], TM, [(i, i + 1) for i in range(n_tm - 1)])
    first = lax.axis_index(TM) == 0
    column = lax.broadcasted_iota(jnp.int32, (1, HALO + width), 1)
    keep = jnp.logical_or(jnp.logical_not(first), column >= HALO)
    hidden = jnp.concatenate([halo, xb], axis=1).astype(jnp.float32)
    for layer in range(LAYERS):
        hb = jnp.where(keep, hidden, 0.0).astype(jnp.bfloat16)
        extended = jnp.concatenate([jnp.zeros((K, D_MAX), jnp.bfloat16), hb], axis=1)
        past = lax.dynamic_slice_in_dim(extended, D_MAX - dilations[layer], HALO + width, 1)
        hidden = conv_layer(hidden, hb, past, conv_w[layer], conv_b[layer])
    target = lax.dynamic_slice_in_dim(hidden[:, HALO:], lax.axis_index("series") * rank_part, rank_part, 0)
    basis_new = basis - 0.5 * (grad_x + (basis - target))
    return (factors_new, m_new, v_new, basis_new)


def solution(mesh):
    n_series, n_tm = mesh.devices.shape
    devices = mesh.devices.reshape(n_series, n_tm // (Y_LO * CORES), Y_LO, CORES)
    fine = Mesh(devices, ("series",) + TM)
    block = P("series", TM)
    rows = P(("series",) + TM, None)
    return jax.shard_map(
        on_device,
        mesh=fine,
        in_specs=(block, block, rows, rows, rows, block, P(), P(), P()),
        out_specs=(rows, rows, rows, block),
        check_vma=False,
    )
```

```python
import math

import jax
import jax.numpy as jnp
from jax import lax
from jax.sharding import Mesh
from jax.sharding import PartitionSpec as P

K = 128
TILE = 128
LAYERS = 4
D_MAX = 32
HALO = LAYERS * D_MAX
CORES = 2
Y_LO = 4
TM = ("z", "ylo", "core")
ROW = ("z", "ylo")


def expand(tiles, tile):
    rows, cols = tiles.shape
    ones = tiles.astype(jnp.float32)
    return jnp.broadcast_to(ones[:, None, :, None], (rows, tile, cols, tile)).reshape(
        rows * tile, cols * tile
    )


def adam_update(factors, adam_m, adam_v, grad_f):
    m_new = 0.9 * adam_m + 0.1 * grad_f
    v_new = 0.999 * adam_v + 0.001 * grad_f * grad_f
    m_hat = m_new / (1.0 - 0.9**10)
    v_hat = v_new / (1.0 - 0.999**10)
    return (factors - 0.01 * m_hat / (jnp.sqrt(v_hat) + 1e-08), m_new, v_new)


def conv_layer(hidden, hb, past, weights, biases):
    z_val = jnp.dot(weights[0], past, preferred_element_type=jnp.float32)
    z_val = z_val + jnp.dot(weights[1], hb, preferred_element_type=jnp.float32)
    z_val = z_val + biases[:, None]
    return hidden + jax.nn.relu(z_val)


def gather_by_a2a(x, axis, count):
    copies = jnp.broadcast_to(x[None], (count,) + x.shape)
    return lax.all_to_all(copies, axis, 0, 0, tiled=True)


def on_device(y_obs, tile_mask, factors, adam_m, adam_v, basis, dilations, conv_w, conv_b):
    own_rows = factors.shape[0]
    width = basis.shape[1]
    rank_part = basis.shape[0]
    n_row = lax.axis_size(ROW)
    n_series = lax.axis_size("series")
    n_tm = n_row * CORES
    total_time = width * n_tm
    total_series = own_rows * n_tm * n_series

    fb = factors.astype(jnp.bfloat16)
    f_rows = gather_by_a2a(fb, ROW, n_row)
    f_all = gather_by_a2a(f_rows, "core", CORES)
    f_block = jnp.swapaxes(f_all, 0, 1).reshape(n_tm * own_rows, K)

    x_parts = gather_by_a2a(basis.astype(jnp.bfloat16), "series", n_series)
    x_full = x_parts.reshape(n_series * rank_part, width)

    pred = jnp.dot(f_block, x_full, preferred_element_type=jnp.float32)
    resid = expand(tile_mask, TILE) * (y_obs.astype(jnp.float32) - pred)
    rb = resid.astype(jnp.bfloat16)
    scale_f = 1.0 / math.sqrt(total_time)
    contract_time = (((1,), (1,)), ((), ()))
    partial_f = -lax.dot_general(rb, x_full, contract_time, preferred_element_type=jnp.float32) * scale_f
    by_core = partial_f.reshape(n_row, CORES, own_rows, K)
    by_core = lax.all_to_all(by_core.astype(jnp.bfloat16), "core", 1, 1, tiled=True)
    by_core = by_core.astype(jnp.float32).sum(1)
    by_row = lax.all_to_all(by_core.astype(jnp.bfloat16), ROW, 0, 0, tiled=True)
    grad_f = by_row.astype(jnp.float32).sum(0)
    factors_new, m_new, v_new = adam_update(factors, adam_m, adam_v, grad_f)

    partial_x = -lax.dot_general(
        f_block, rb, (((0,), (0,)), ((), ())), preferred_element_type=jnp.float32
    )
    partial_x = partial_x * math.sqrt(K / total_series)
    pieces = partial_x.reshape(n_series, rank_part, width)
    arrived = lax.all_to_all(pieces.astype(jnp.bfloat16), "series", 0, 0, tiled=True)
    grad_x = arrived.astype(jnp.float32).sum(0)

    xb = x_full
    halo = lax.ppermute(xb[:, width - HALO :], TM, [(i, i + 1) for i in range(n_tm - 1)])
    first = lax.axis_index(TM) == 0
    column = lax.broadcasted_iota(jnp.int32, (1, HALO + width), 1)
    keep = jnp.logical_or(jnp.logical_not(first), column >= HALO)
    hidden = jnp.concatenate([halo, xb], axis=1).astype(jnp.float32)
    for layer in range(LAYERS):
        hb = jnp.where(keep, hidden, 0.0).astype(jnp.bfloat16)
        extended = jnp.concatenate([jnp.zeros((K, D_MAX), jnp.bfloat16), hb], axis=1)
        past = lax.dynamic_slice_in_dim(extended, D_MAX - dilations[layer], HALO + width, 1)
        hidden = conv_layer(hidden, hb, past, conv_w[layer], conv_b[layer])
    target = lax.dynamic_slice_in_dim(hidden[:, HALO:], lax.axis_index("series") * rank_part, rank_part, 0)
    basis_new = basis - 0.5 * (grad_x + (basis - target))
    return (factors_new, m_new, v_new, basis_new)


def solution(mesh):
    n_series, n_tm = mesh.devices.shape
    devices = mesh.devices.reshape(n_series, n_tm // (Y_LO * CORES), Y_LO, CORES)
    fine = Mesh(devices, ("series",) + TM)
    block = P("series", TM)
    rows = P(("series",) + TM, None)
    return jax.shard_map(
        on_device,
        mesh=fine,
        in_specs=(block, block, rows, rows, rows, block, P(), P(), P()),
        out_specs=(rows, rows, rows, block),
        check_vma=False,
    )
```

```python
import math

import jax
import jax.numpy as jnp
from jax import lax
from jax.sharding import Mesh
from jax.sharding import PartitionSpec as P

K = 128
TILE = 128
LAYERS = 4
D_MAX = 32
HALO = LAYERS * D_MAX
CORES = 2
Y_LO = 4
TM = ("z", "ylo", "core")
ROW = ("z", "ylo")


def expand(tiles, tile):
    rows, cols = tiles.shape
    ones = tiles.astype(jnp.float32)
    return jnp.broadcast_to(ones[:, None, :, None], (rows, tile, cols, tile)).reshape(
        rows * tile, cols * tile
    )


def adam_update(factors, adam_m, adam_v, grad_f):
    m_new = 0.9 * adam_m + 0.1 * grad_f
    v_new = 0.999 * adam_v + 0.001 * grad_f * grad_f
    m_hat = m_new / (1.0 - 0.9**10)
    v_hat = v_new / (1.0 - 0.999**10)
    return (factors - 0.01 * m_hat / (jnp.sqrt(v_hat) + 1e-08), m_new, v_new)


def conv_layer(hidden, hb, past, weights, biases):
    z_val = jnp.dot(weights[0], past, preferred_element_type=jnp.float32)
    z_val = z_val + jnp.dot(weights[1], hb, preferred_element_type=jnp.float32)
    z_val = z_val + biases[:, None]
    return hidden + jax.nn.relu(z_val)


def gather_by_a2a(x, axis, count):
    copies = jnp.broadcast_to(x[None], (count,) + x.shape)
    return lax.all_to_all(copies, axis, 0, 0, tiled=True)


def on_device(y_obs, tile_mask, factors, adam_m, adam_v, basis, dilations, conv_w, conv_b):
    own_rows = factors.shape[0]
    width = basis.shape[1]
    rank_part = basis.shape[0]
    n_row = lax.axis_size(ROW)
    n_series = lax.axis_size("series")
    n_tm = n_row * CORES
    total_time = width * n_tm
    total_series = own_rows * n_tm * n_series

    fb = factors.astype(jnp.bfloat16)
    f_rows = gather_by_a2a(fb, ROW, n_row)
    core = lax.axis_index("core")
    f_other = lax.ppermute(f_rows, "core", [(0, 1), (1, 0)])
    low = core == 0
    f_block = jnp.stack(
        [jnp.where(low, f_rows, f_other), jnp.where(low, f_other, f_rows)], axis=1
    ).reshape(n_tm * own_rows, K)

    x_parts = gather_by_a2a(basis.astype(jnp.bfloat16), "series", n_series)
    x_full = x_parts.reshape(n_series * rank_part, width)

    pred = jnp.dot(f_block, x_full, preferred_element_type=jnp.float32)
    resid = expand(tile_mask, TILE) * (y_obs.astype(jnp.float32) - pred)
    rb = resid.astype(jnp.bfloat16)
    scale_f = 1.0 / math.sqrt(total_time)
    contract_time = (((1,), (1,)), ((), ()))
    partial_f = -lax.dot_general(rb, x_full, contract_time, preferred_element_type=jnp.float32) * scale_f
    by_core = partial_f.reshape(n_row, CORES, own_rows, K)
    kept = lax.dynamic_index_in_dim(by_core, core, 1, keepdims=False)
    given = lax.dynamic_index_in_dim(by_core, 1 - core, 1, keepdims=False)
    by_core = kept + lax.ppermute(given.astype(jnp.bfloat16), "core", [(0, 1), (1, 0)]).astype(jnp.float32)
    by_row = lax.all_to_all(by_core.astype(jnp.bfloat16), ROW, 0, 0, tiled=True)
    grad_f = by_row.astype(jnp.float32).sum(0)
    factors_new, m_new, v_new = adam_update(factors, adam_m, adam_v, grad_f)

    partial_x = -lax.dot_general(
        f_block, rb, (((0,), (0,)), ((), ())), preferred_element_type=jnp.float32
    )
    partial_x = partial_x * math.sqrt(K / total_series)
    pieces = partial_x.reshape(n_series, rank_part, width)
    arrived = lax.all_to_all(pieces.astype(jnp.bfloat16), "series", 0, 0, tiled=True)
    grad_x = arrived.astype(jnp.float32).sum(0)

    xb = x_full
    halo = lax.ppermute(xb[:, width - HALO :], TM, [(i, i + 1) for i in range(n_tm - 1)])
    first = lax.axis_index(TM) == 0
    column = lax.broadcasted_iota(jnp.int32, (1, HALO + width), 1)
    keep = jnp.logical_or(jnp.logical_not(first), column >= HALO)
    hidden = jnp.concatenate([halo, xb], axis=1).astype(jnp.float32)
    for layer in range(LAYERS):
        hb = jnp.where(keep, hidden, 0.0).astype(jnp.bfloat16)
        extended = jnp.concatenate([jnp.zeros((K, D_MAX), jnp.bfloat16), hb], axis=1)
        past = lax.dynamic_slice_in_dim(extended, D_MAX - dilations[layer], HALO + width, 1)
        hidden = conv_layer(hidden, hb, past, conv_w[layer], conv_b[layer])
    target = lax.dynamic_slice_in_dim(hidden[:, HALO:], lax.axis_index("series") * rank_part, rank_part, 0)
    basis_new = basis - 0.5 * (grad_x + (basis - target))
    return (factors_new, m_new, v_new, basis_new)


def solution(mesh):
    n_series, n_tm = mesh.devices.shape
    devices = mesh.devices.reshape(n_series, n_tm // (Y_LO * CORES), Y_LO, CORES)
    fine = Mesh(devices, ("series",) + TM)
    block = P("series", TM)
    rows = P(("series",) + TM, None)
    return jax.shard_map(
        on_device,
        mesh=fine,
        in_specs=(block, block, rows, rows, rows, block, P(), P(), P()),
        out_specs=(rows, rows, rows, block),
        check_vma=False,
    )
```

```python
import math

import jax
import jax.numpy as jnp
from jax import lax
from jax.sharding import Mesh
from jax.sharding import PartitionSpec as P

K = 128
TILE = 128
LAYERS = 4
D_MAX = 32
HALO = LAYERS * D_MAX
CORES = 2
Y_LO = 4
TM = ("z", "ylo", "core")
ROW = ("z", "ylo")


def expand(tiles, tile):
    rows, cols = tiles.shape
    ones = tiles.astype(jnp.float32)
    return jnp.broadcast_to(ones[:, None, :, None], (rows, tile, cols, tile)).reshape(
        rows * tile, cols * tile
    )


def adam_update(factors, adam_m, adam_v, grad_f):
    m_new = 0.9 * adam_m + 0.1 * grad_f
    v_new = 0.999 * adam_v + 0.001 * grad_f * grad_f
    m_hat = m_new / (1.0 - 0.9**10)
    v_hat = v_new / (1.0 - 0.999**10)
    return (factors - 0.01 * m_hat / (jnp.sqrt(v_hat) + 1e-08), m_new, v_new)


def conv_layer(hidden, hb, past, weights, biases):
    z_val = jnp.dot(weights[0], past, preferred_element_type=jnp.float32)
    z_val = z_val + jnp.dot(weights[1], hb, preferred_element_type=jnp.float32)
    z_val = z_val + biases[:, None]
    return hidden + jax.nn.relu(z_val)


def gather_by_a2a(x, axis, count):
    copies = jnp.broadcast_to(x[None], (count,) + x.shape)
    return lax.all_to_all(copies, axis, 0, 0, tiled=True)


def on_device(y_obs, tile_mask, factors, adam_m, adam_v, basis, dilations, conv_w, conv_b):
    own_rows = factors.shape[0]
    width = basis.shape[1]
    rank_part = basis.shape[0]
    n_row = lax.axis_size(ROW)
    n_series = lax.axis_size("series")
    n_tm = n_row * CORES
    total_time = width * n_tm
    total_series = own_rows * n_tm * n_series

    fb = factors.astype(jnp.bfloat16)
    f_rows = gather_by_a2a(fb, ROW, n_row)
    f_all = gather_by_a2a(f_rows, "core", CORES)
    f_block = jnp.swapaxes(f_all, 0, 1).reshape(n_tm * own_rows, K)

    x_parts = gather_by_a2a(basis.astype(jnp.bfloat16), "series", n_series)
    x_full = x_parts.reshape(n_series * rank_part, width)

    pred = jnp.dot(f_block, x_full, preferred_element_type=jnp.float32)
    tiles = tile_mask.shape[0]
    mask_cols = jnp.repeat(tile_mask.astype(jnp.float32), TILE, axis=1)
    gap = (y_obs.astype(jnp.float32) - pred).reshape(tiles, TILE, width)
    resid = (mask_cols[:, None, :] * gap).reshape(tiles * TILE, width)
    rb = resid.astype(jnp.bfloat16)
    scale_f = 1.0 / math.sqrt(total_time)
    contract_time = (((1,), (1,)), ((), ()))
    partial_f = -lax.dot_general(rb, x_full, contract_time, preferred_element_type=jnp.float32) * scale_f
    by_core = partial_f.reshape(n_row, CORES, own_rows, K)
    by_core = lax.all_to_all(by_core.astype(jnp.bfloat16), "core", 1, 1, tiled=True)
    by_core = by_core.astype(jnp.float32).sum(1)
    by_row = lax.all_to_all(by_core.astype(jnp.bfloat16), ROW, 0, 0, tiled=True)
    grad_f = by_row.astype(jnp.float32).sum(0)
    factors_new, m_new, v_new = adam_update(factors, adam_m, adam_v, grad_f)

    partial_x = -lax.dot_general(
        f_block, rb, (((0,), (0,)), ((), ())), preferred_element_type=jnp.float32
    )
    partial_x = partial_x * math.sqrt(K / total_series)
    pieces = partial_x.reshape(n_series, rank_part, width)
    arrived = lax.all_to_all(pieces.astype(jnp.bfloat16), "series", 0, 0, tiled=True)
    grad_x = arrived.astype(jnp.float32).sum(0)

    xb = x_full
    halo = lax.ppermute(xb[:, width - HALO :], TM, [(i, i + 1) for i in range(n_tm - 1)])
    first = lax.axis_index(TM) == 0
    column = lax.broadcasted_iota(jnp.int32, (1, HALO + width), 1)
    keep = jnp.logical_or(jnp.logical_not(first), column >= HALO)
    hidden = jnp.concatenate([halo, xb], axis=1).astype(jnp.float32)
    for layer in range(LAYERS):
        hb = jnp.where(keep, hidden, 0.0).astype(jnp.bfloat16)
        extended = jnp.concatenate([jnp.zeros((K, D_MAX), jnp.bfloat16), hb], axis=1)
        past = lax.dynamic_slice_in_dim(extended, D_MAX - dilations[layer], HALO + width, 1)
        hidden = conv_layer(hidden, hb, past, conv_w[layer], conv_b[layer])
    target = lax.dynamic_slice_in_dim(hidden[:, HALO:], lax.axis_index("series") * rank_part, rank_part, 0)
    basis_new = basis - 0.5 * (grad_x + (basis - target))
    return (factors_new, m_new, v_new, basis_new)


def solution(mesh):
    n_series, n_tm = mesh.devices.shape
    devices = mesh.devices.reshape(n_series, n_tm // (Y_LO * CORES), Y_LO, CORES)
    fine = Mesh(devices, ("series",) + TM)
    block = P("series", TM)
    rows = P(("series",) + TM, None)
    return jax.shard_map(
        on_device,
        mesh=fine,
        in_specs=(block, block, rows, rows, rows, block, P(), P(), P()),
        out_specs=(rows, rows, rows, block),
        check_vma=False,
    )
```

```python
import math

import jax
import jax.numpy as jnp
from jax import lax
from jax.experimental import pallas as pl
from jax.experimental.pallas import tpu as pltpu
from jax.sharding import Mesh
from jax.sharding import PartitionSpec as P

K = 128
TILE = 128
LAYERS = 4
D_MAX = 32
HALO = LAYERS * D_MAX
CORES = 2
Y_LO = 4
TM = ("z", "ylo", "core")
ROW = ("z", "ylo")


def expand(tiles, tile):
    rows, cols = tiles.shape
    ones = tiles.astype(jnp.float32)
    return jnp.broadcast_to(ones[:, None, :, None], (rows, tile, cols, tile)).reshape(
        rows * tile, cols * tile
    )


def adam_update(factors, adam_m, adam_v, grad_f):
    m_new = 0.9 * adam_m + 0.1 * grad_f
    v_new = 0.999 * adam_v + 0.001 * grad_f * grad_f
    m_hat = m_new / (1.0 - 0.9**10)
    v_hat = v_new / (1.0 - 0.999**10)
    return (factors - 0.01 * m_hat / (jnp.sqrt(v_hat) + 1e-08), m_new, v_new)


def conv_layer(hidden, hb, past, weights, biases):
    z_val = jnp.dot(weights[0], past, preferred_element_type=jnp.float32)
    z_val = z_val + jnp.dot(weights[1], hb, preferred_element_type=jnp.float32)
    z_val = z_val + biases[:, None]
    return hidden + jax.nn.relu(z_val)


def gather_by_a2a(x, axis, count):
    copies = jnp.broadcast_to(x[None], (count,) + x.shape)
    return lax.all_to_all(copies, axis, 0, 0, tiled=True)


def residual_kernel(scale_f, y_ref, m_ref, f_ref, x_ref, pf_ref, px_ref):
    step = pl.program_id(0)
    rows, width = y_ref.shape
    f = f_ref[...]
    x = x_ref[...]
    pred = jnp.dot(f, x, preferred_element_type=jnp.float32)
    gap = (y_ref[...].astype(jnp.float32) - pred).reshape(rows // TILE, TILE, width)
    rb = (m_ref[...][:, None, :] * gap).reshape(rows, width).astype(jnp.bfloat16)
    contract_time = (((1,), (1,)), ((), ()))
    pf_ref[...] = -lax.dot_general(rb, x, contract_time, preferred_element_type=jnp.float32) * scale_f
    part = lax.dot_general(f, rb, (((0,), (0,)), ((), ())), preferred_element_type=jnp.float32)

    @pl.when(step == 0)
    def _():
        px_ref[...] = part

    @pl.when(step > 0)
    def _():
        px_ref[...] += part


def residual_products(y_obs, mask_cols, f_block, x_full, scale_f):
    n_rows, width = y_obs.shape
    block = 8 * TILE
    steps = n_rows // block
    kernel = lambda *refs: residual_kernel(scale_f, *refs)
    flops = 3 * 2 * n_rows * width * K
    moved = n_rows * width * 2 + n_rows * K * 2 + n_rows * K * 4 + 2 * K * width * 4
    return pl.pallas_call(
        kernel,
        grid=(steps,),
        in_specs=[
            pl.BlockSpec((block, width), lambda i: (i, 0)),
            pl.BlockSpec((block // TILE, width), lambda i: (i, 0)),
            pl.BlockSpec((block, K), lambda i: (i, 0)),
            pl.BlockSpec((K, width), lambda i: (0, 0)),
        ],
        out_specs=[
            pl.BlockSpec((block, K), lambda i: (i, 0)),
            pl.BlockSpec((K, width), lambda i: (0, 0)),
        ],
        out_shape=[
            jax.ShapeDtypeStruct((n_rows, K), jnp.float32),
            jax.ShapeDtypeStruct((K, width), jnp.float32),
        ],
        compiler_params=pltpu.CompilerParams(dimension_semantics=("arbitrary",)),
        cost_estimate=pl.CostEstimate(flops=flops, bytes_accessed=moved, transcendentals=0),
    )(y_obs, mask_cols, f_block, x_full)


def on_device(y_obs, tile_mask, factors, adam_m, adam_v, basis, dilations, conv_w, conv_b):
    own_rows = factors.shape[0]
    width = basis.shape[1]
    rank_part = basis.shape[0]
    n_row = lax.axis_size(ROW)
    n_series = lax.axis_size("series")
    n_tm = n_row * CORES
    total_time = width * n_tm
    total_series = own_rows * n_tm * n_series

    fb = factors.astype(jnp.bfloat16)
    f_rows = gather_by_a2a(fb, ROW, n_row)
    f_all = gather_by_a2a(f_rows, "core", CORES)
    f_block = jnp.swapaxes(f_all, 0, 1).reshape(n_tm * own_rows, K)

    x_parts = gather_by_a2a(basis.astype(jnp.bfloat16), "series", n_series)
    x_full = x_parts.reshape(n_series * rank_part, width)

    mask_cols = jnp.repeat(tile_mask.astype(jnp.float32), TILE, axis=1)
    scale_f = 1.0 / math.sqrt(total_time)
    partial_f, product_x = residual_products(y_obs, mask_cols, f_block, x_full, scale_f)
    by_core = partial_f.reshape(n_row, CORES, own_rows, K)
    by_core = lax.all_to_all(by_core.astype(jnp.bfloat16), "core", 1, 1, tiled=True)
    by_core = by_core.astype(jnp.float32).sum(1)
    by_row = lax.all_to_all(by_core.astype(jnp.bfloat16), ROW, 0, 0, tiled=True)
    grad_f = by_row.astype(jnp.float32).sum(0)
    factors_new, m_new, v_new = adam_update(factors, adam_m, adam_v, grad_f)

    partial_x = -product_x * math.sqrt(K / total_series)
    pieces = partial_x.reshape(n_series, rank_part, width)
    arrived = lax.all_to_all(pieces.astype(jnp.bfloat16), "series", 0, 0, tiled=True)
    grad_x = arrived.astype(jnp.float32).sum(0)

    xb = x_full
    halo = lax.ppermute(xb[:, width - HALO :], TM, [(i, i + 1) for i in range(n_tm - 1)])
    first = lax.axis_index(TM) == 0
    column = lax.broadcasted_iota(jnp.int32, (1, HALO + width), 1)
    keep = jnp.logical_or(jnp.logical_not(first), column >= HALO)
    hidden = jnp.concatenate([halo, xb], axis=1).astype(jnp.float32)
    for layer in range(LAYERS):
        hb = jnp.where(keep, hidden, 0.0).astype(jnp.bfloat16)
        extended = jnp.concatenate([jnp.zeros((K, D_MAX), jnp.bfloat16), hb], axis=1)
        past = lax.dynamic_slice_in_dim(extended, D_MAX - dilations[layer], HALO + width, 1)
        hidden = conv_layer(hidden, hb, past, conv_w[layer], conv_b[layer])
    target = lax.dynamic_slice_in_dim(hidden[:, HALO:], lax.axis_index("series") * rank_part, rank_part, 0)
    basis_new = basis - 0.5 * (grad_x + (basis - target))
    return (factors_new, m_new, v_new, basis_new)


def solution(mesh):
    n_series, n_tm = mesh.devices.shape
    devices = mesh.devices.reshape(n_series, n_tm // (Y_LO * CORES), Y_LO, CORES)
    fine = Mesh(devices, ("series",) + TM)
    block = P("series", TM)
    rows = P(("series",) + TM, None)
    return jax.shard_map(
        on_device,
        mesh=fine,
        in_specs=(block, block, rows, rows, rows, block, P(), P(), P()),
        out_specs=(rows, rows, rows, block),
        check_vma=False,
    )
```

```python
import math

import jax
import jax.numpy as jnp
from jax import lax
from jax.sharding import Mesh
from jax.sharding import PartitionSpec as P

K = 128
TILE = 128
LAYERS = 4
D_MAX = 32
HALO = LAYERS * D_MAX
CORES = 2
Y_LO = 4
TM = ("z", "ylo", "core")
ROW = ("z", "ylo")


def expand(tiles, tile):
    rows, cols = tiles.shape
    ones = tiles.astype(jnp.float32)
    return jnp.broadcast_to(ones[:, None, :, None], (rows, tile, cols, tile)).reshape(
        rows * tile, cols * tile
    )


def adam_update(factors, adam_m, adam_v, grad_f):
    m_new = 0.9 * adam_m + 0.1 * grad_f
    v_new = 0.999 * adam_v + 0.001 * grad_f * grad_f
    m_hat = m_new / (1.0 - 0.9**10)
    v_hat = v_new / (1.0 - 0.999**10)
    return (factors - 0.01 * m_hat / (jnp.sqrt(v_hat) + 1e-08), m_new, v_new)


def conv_layer(hidden, hb, past, weights, biases):
    z_val = jnp.dot(weights[0], past, preferred_element_type=jnp.float32)
    z_val = z_val + jnp.dot(weights[1], hb, preferred_element_type=jnp.float32)
    z_val = z_val + biases[:, None]
    return hidden + jax.nn.relu(z_val)


def gather_by_a2a(x, axis, count):
    copies = jnp.broadcast_to(x[None], (count,) + x.shape)
    return lax.all_to_all(copies, axis, 0, 0, tiled=True)


def on_device(y_obs, tile_mask, factors, adam_m, adam_v, basis, dilations, conv_w, conv_b):
    own_rows = factors.shape[0]
    width = basis.shape[1]
    rank_part = basis.shape[0]
    n_row = lax.axis_size(ROW)
    n_series = lax.axis_size("series")
    n_tm = n_row * CORES
    total_time = width * n_tm
    total_series = own_rows * n_tm * n_series

    fb = factors.astype(jnp.bfloat16)
    f_rows = gather_by_a2a(fb, ROW, n_row)
    x_copies = jnp.broadcast_to(basis.astype(jnp.bfloat16)[None], (n_series,) + basis.shape)
    f_rows, x_copies = lax.optimization_barrier((f_rows, x_copies))
    x_parts = lax.all_to_all(x_copies, "series", 0, 0, tiled=True)
    x_full = x_parts.reshape(n_series * rank_part, width)
    f_all = gather_by_a2a(f_rows, "core", CORES)
    f_block = jnp.swapaxes(f_all, 0, 1).reshape(n_tm * own_rows, K)

    pred = jnp.dot(f_block, x_full, preferred_element_type=jnp.float32)
    tiles = tile_mask.shape[0]
    mask_cols = jnp.repeat(tile_mask.astype(jnp.float32), TILE, axis=1)
    gap = (y_obs.astype(jnp.float32) - pred).reshape(tiles, TILE, width)
    resid = (mask_cols[:, None, :] * gap).reshape(tiles * TILE, width)
    rb = resid.astype(jnp.bfloat16)
    scale_f = 1.0 / math.sqrt(total_time)
    contract_time = (((1,), (1,)), ((), ()))
    partial_f = -lax.dot_general(rb, x_full, contract_time, preferred_element_type=jnp.float32) * scale_f
    by_core = partial_f.reshape(n_row, CORES, own_rows, K)
    by_core = lax.all_to_all(by_core.astype(jnp.bfloat16), "core", 1, 1, tiled=True)
    by_core = by_core.astype(jnp.float32).sum(1)
    by_row = lax.all_to_all(by_core.astype(jnp.bfloat16), ROW, 0, 0, tiled=True)
    grad_f = by_row.astype(jnp.float32).sum(0)
    factors_new, m_new, v_new = adam_update(factors, adam_m, adam_v, grad_f)

    partial_x = -lax.dot_general(
        f_block, rb, (((0,), (0,)), ((), ())), preferred_element_type=jnp.float32
    )
    partial_x = partial_x * math.sqrt(K / total_series)
    pieces = partial_x.reshape(n_series, rank_part, width)
    arrived = lax.all_to_all(pieces.astype(jnp.bfloat16), "series", 0, 0, tiled=True)
    grad_x = arrived.astype(jnp.float32).sum(0)

    xb = x_full
    halo = lax.ppermute(xb[:, width - HALO :], TM, [(i, i + 1) for i in range(n_tm - 1)])
    first = lax.axis_index(TM) == 0
    column = lax.broadcasted_iota(jnp.int32, (1, HALO + width), 1)
    keep = jnp.logical_or(jnp.logical_not(first), column >= HALO)
    hidden = jnp.concatenate([halo, xb], axis=1).astype(jnp.float32)
    for layer in range(LAYERS):
        hb = jnp.where(keep, hidden, 0.0).astype(jnp.bfloat16)
        extended = jnp.concatenate([jnp.zeros((K, D_MAX), jnp.bfloat16), hb], axis=1)
        past = lax.dynamic_slice_in_dim(extended, D_MAX - dilations[layer], HALO + width, 1)
        hidden = conv_layer(hidden, hb, past, conv_w[layer], conv_b[layer])
    target = lax.dynamic_slice_in_dim(hidden[:, HALO:], lax.axis_index("series") * rank_part, rank_part, 0)
    basis_new = basis - 0.5 * (grad_x + (basis - target))
    return (factors_new, m_new, v_new, basis_new)


def solution(mesh):
    n_series, n_tm = mesh.devices.shape
    devices = mesh.devices.reshape(n_series, n_tm // (Y_LO * CORES), Y_LO, CORES)
    fine = Mesh(devices, ("series",) + TM)
    block = P("series", TM)
    rows = P(("series",) + TM, None)
    return jax.shard_map(
        on_device,
        mesh=fine,
        in_specs=(block, block, rows, rows, rows, block, P(), P(), P()),
        out_specs=(rows, rows, rows, block),
        check_vma=False,
    )
```

```python
import math

import jax
import jax.numpy as jnp
from jax import lax
from jax.sharding import Mesh
from jax.sharding import PartitionSpec as P

K = 128
TILE = 128
LAYERS = 4
D_MAX = 32
HALO = LAYERS * D_MAX
CORES = 2
Y_LO = 4
TM = ("z", "ylo", "core")
ROW = ("z", "ylo")


def expand(tiles, tile):
    rows, cols = tiles.shape
    ones = tiles.astype(jnp.float32)
    return jnp.broadcast_to(ones[:, None, :, None], (rows, tile, cols, tile)).reshape(
        rows * tile, cols * tile
    )


def adam_update(factors, adam_m, adam_v, grad_f):
    m_new = 0.9 * adam_m + 0.1 * grad_f
    v_new = 0.999 * adam_v + 0.001 * grad_f * grad_f
    m_hat = m_new / (1.0 - 0.9**10)
    v_hat = v_new / (1.0 - 0.999**10)
    return (factors - 0.01 * m_hat / (jnp.sqrt(v_hat) + 1e-08), m_new, v_new)


def conv_layer(hidden, hb, past, weights, biases):
    z_val = jnp.dot(weights[0], past, preferred_element_type=jnp.float32)
    z_val = z_val + jnp.dot(weights[1], hb, preferred_element_type=jnp.float32)
    z_val = z_val + biases[:, None]
    return hidden + jax.nn.relu(z_val)


def gather_by_a2a(x, axis, count):
    copies = jnp.broadcast_to(x[None], (count,) + x.shape)
    return lax.all_to_all(copies, axis, 0, 0, tiled=True)


def on_device(y_obs, tile_mask, factors, adam_m, adam_v, basis, dilations, conv_w, conv_b):
    own_rows = factors.shape[0]
    width = basis.shape[1]
    rank_part = basis.shape[0]
    n_row = lax.axis_size(ROW)
    n_series = lax.axis_size("series")
    n_tm = n_row * CORES
    total_time = width * n_tm
    total_series = own_rows * n_tm * n_series

    fb = factors.astype(jnp.bfloat16)
    f_rows = gather_by_a2a(fb, ROW, n_row)
    f_all = gather_by_a2a(f_rows, "core", CORES)
    f_block = jnp.swapaxes(f_all, 0, 1).reshape(n_tm * own_rows, K)

    x_parts = gather_by_a2a(basis.astype(jnp.bfloat16), "series", n_series)
    x_full = x_parts.reshape(n_series * rank_part, width)

    pred = jnp.dot(f_block, x_full, preferred_element_type=jnp.float32)
    tiles = tile_mask.shape[0]
    mask_cols = jnp.repeat(tile_mask.astype(jnp.float32), TILE, axis=1)
    gap = (y_obs.astype(jnp.float32) - pred).reshape(tiles, TILE, width)
    resid = (mask_cols[:, None, :] * gap).reshape(tiles * TILE, width)
    rb = resid.astype(jnp.bfloat16)
    scale_f = 1.0 / math.sqrt(total_time)
    contract_time = (((1,), (1,)), ((), ()))
    partial_f = -lax.dot_general(rb, x_full, contract_time, preferred_element_type=jnp.float32) * scale_f
    by_core = partial_f.reshape(n_row, CORES, own_rows, K)
    core = lax.axis_index("core")
    kept = lax.dynamic_index_in_dim(by_core, core, 1, keepdims=False)
    given = lax.dynamic_index_in_dim(by_core, 1 - core, 1, keepdims=False)
    by_core = kept + lax.ppermute(given.astype(jnp.bfloat16), "core", [(0, 1), (1, 0)]).astype(jnp.float32)
    by_row = lax.all_to_all(by_core.astype(jnp.bfloat16), ROW, 0, 0, tiled=True)
    grad_f = by_row.astype(jnp.float32).sum(0)
    factors_new, m_new, v_new = adam_update(factors, adam_m, adam_v, grad_f)

    partial_x = -lax.dot_general(
        f_block, rb, (((0,), (0,)), ((), ())), preferred_element_type=jnp.float32
    )
    partial_x = partial_x * math.sqrt(K / total_series)
    pieces = partial_x.reshape(n_series, rank_part, width)
    arrived = lax.all_to_all(pieces.astype(jnp.bfloat16), "series", 0, 0, tiled=True)
    grad_x = arrived.astype(jnp.float32).sum(0)

    xb = x_full
    halo = lax.ppermute(xb[:, width - HALO :], TM, [(i, i + 1) for i in range(n_tm - 1)])
    first = lax.axis_index(TM) == 0
    column = lax.broadcasted_iota(jnp.int32, (1, HALO + width), 1)
    keep = jnp.logical_or(jnp.logical_not(first), column >= HALO)
    hidden = jnp.concatenate([halo, xb], axis=1).astype(jnp.float32)
    for layer in range(LAYERS):
        hb = jnp.where(keep, hidden, 0.0).astype(jnp.bfloat16)
        extended = jnp.concatenate([jnp.zeros((K, D_MAX), jnp.bfloat16), hb], axis=1)
        past = lax.dynamic_slice_in_dim(extended, D_MAX - dilations[layer], HALO + width, 1)
        hidden = conv_layer(hidden, hb, past, conv_w[layer], conv_b[layer])
    target = lax.dynamic_slice_in_dim(hidden[:, HALO:], lax.axis_index("series") * rank_part, rank_part, 0)
    basis_new = basis - 0.5 * (grad_x + (basis - target))
    return (factors_new, m_new, v_new, basis_new)


def solution(mesh):
    n_series, n_tm = mesh.devices.shape
    devices = mesh.devices.reshape(n_series, n_tm // (Y_LO * CORES), Y_LO, CORES)
    fine = Mesh(devices, ("series",) + TM)
    block = P("series", TM)
    rows = P(("series",) + TM, None)
    return jax.shard_map(
        on_device,
        mesh=fine,
        in_specs=(block, block, rows, rows, rows, block, P(), P(), P()),
        out_specs=(rows, rows, rows, block),
        check_vma=False,
    )
```

```python
import math

import jax
import jax.numpy as jnp
from jax import lax
from jax.sharding import Mesh
from jax.sharding import PartitionSpec as P

K = 128
TILE = 128
LAYERS = 4
D_MAX = 32
HALO = LAYERS * D_MAX
CORES = 2
Y_LO = 4
TM = ("z", "ylo", "core")
ROW = ("z", "ylo")


def expand(tiles, tile):
    rows, cols = tiles.shape
    ones = tiles.astype(jnp.float32)
    return jnp.broadcast_to(ones[:, None, :, None], (rows, tile, cols, tile)).reshape(
        rows * tile, cols * tile
    )


def adam_update(factors, adam_m, adam_v, grad_f):
    m_new = 0.9 * adam_m + 0.1 * grad_f
    v_new = 0.999 * adam_v + 0.001 * grad_f * grad_f
    m_hat = m_new / (1.0 - 0.9**10)
    v_hat = v_new / (1.0 - 0.999**10)
    return (factors - 0.01 * m_hat / (jnp.sqrt(v_hat) + 1e-08), m_new, v_new)


def conv_layer(hidden, hb, past, weights, biases):
    z_val = jnp.dot(weights[0], past, preferred_element_type=jnp.float32)
    z_val = z_val + jnp.dot(weights[1], hb, preferred_element_type=jnp.float32)
    z_val = z_val + biases[:, None]
    return hidden + jax.nn.relu(z_val)


def gather_by_a2a(x, axis, count):
    copies = jnp.broadcast_to(x[None], (count,) + x.shape)
    return lax.all_to_all(copies, axis, 0, 0, tiled=True)


def on_device(y_obs, tile_mask, factors, adam_m, adam_v, basis, dilations, conv_w, conv_b):
    own_rows = factors.shape[0]
    width = basis.shape[1]
    rank_part = basis.shape[0]
    n_row = lax.axis_size(ROW)
    n_series = lax.axis_size("series")
    n_tm = n_row * CORES
    total_time = width * n_tm
    total_series = own_rows * n_tm * n_series

    fb = factors.astype(jnp.bfloat16)
    f_rows = gather_by_a2a(fb, ROW, n_row)
    core = lax.axis_index("core")
    f_other = lax.ppermute(f_rows, "core", [(0, 1), (1, 0)])

    x_parts = gather_by_a2a(basis.astype(jnp.bfloat16), "series", n_series)
    x_full = x_parts.reshape(n_series * rank_part, width)

    tiles = tile_mask.shape[0]
    mask_cols = jnp.repeat(tile_mask.astype(jnp.float32), TILE, axis=1)
    scale_f = 1.0 / math.sqrt(total_time)
    contract_time = (((1,), (1,)), ((), ()))
    y_rows = y_obs.reshape(n_row, CORES, own_rows, width)

    def half(f_half, owner):
        f2 = f_half.reshape(n_row * own_rows, K)
        y_half = lax.dynamic_index_in_dim(y_rows, owner, 1, keepdims=False)
        pred = jnp.dot(f2, x_full, preferred_element_type=jnp.float32).reshape(n_row, own_rows, width)
        gap = y_half.astype(jnp.float32) - pred
        rb = (mask_cols[:, None, :] * gap).reshape(n_row * own_rows, width).astype(jnp.bfloat16)
        part_f = -lax.dot_general(rb, x_full, contract_time, preferred_element_type=jnp.float32) * scale_f
        part_x = lax.dot_general(f2, rb, (((0,), (0,)), ((), ())), preferred_element_type=jnp.float32)
        return part_f.reshape(n_row, own_rows, K), part_x

    kept, x_mine = half(f_rows, core)
    given, x_theirs = half(f_other, 1 - core)
    by_core = kept + lax.ppermute(given.astype(jnp.bfloat16), "core", [(0, 1), (1, 0)]).astype(jnp.float32)
    by_row = lax.all_to_all(by_core.astype(jnp.bfloat16), ROW, 0, 0, tiled=True)
    grad_f = by_row.astype(jnp.float32).sum(0)
    factors_new, m_new, v_new = adam_update(factors, adam_m, adam_v, grad_f)

    partial_x = -(x_mine + x_theirs) * math.sqrt(K / total_series)
    pieces = partial_x.reshape(n_series, rank_part, width)
    arrived = lax.all_to_all(pieces.astype(jnp.bfloat16), "series", 0, 0, tiled=True)
    grad_x = arrived.astype(jnp.float32).sum(0)

    xb = x_full
    halo = lax.ppermute(xb[:, width - HALO :], TM, [(i, i + 1) for i in range(n_tm - 1)])
    first = lax.axis_index(TM) == 0
    column = lax.broadcasted_iota(jnp.int32, (1, HALO + width), 1)
    keep = jnp.logical_or(jnp.logical_not(first), column >= HALO)
    hidden = jnp.concatenate([halo, xb], axis=1).astype(jnp.float32)
    for layer in range(LAYERS):
        hb = jnp.where(keep, hidden, 0.0).astype(jnp.bfloat16)
        extended = jnp.concatenate([jnp.zeros((K, D_MAX), jnp.bfloat16), hb], axis=1)
        past = lax.dynamic_slice_in_dim(extended, D_MAX - dilations[layer], HALO + width, 1)
        hidden = conv_layer(hidden, hb, past, conv_w[layer], conv_b[layer])
    target = lax.dynamic_slice_in_dim(hidden[:, HALO:], lax.axis_index("series") * rank_part, rank_part, 0)
    basis_new = basis - 0.5 * (grad_x + (basis - target))
    return (factors_new, m_new, v_new, basis_new)


def solution(mesh):
    n_series, n_tm = mesh.devices.shape
    devices = mesh.devices.reshape(n_series, n_tm // (Y_LO * CORES), Y_LO, CORES)
    fine = Mesh(devices, ("series",) + TM)
    block = P("series", TM)
    rows = P(("series",) + TM, None)
    return jax.shard_map(
        on_device,
        mesh=fine,
        in_specs=(block, block, rows, rows, rows, block, P(), P(), P()),
        out_specs=(rows, rows, rows, block),
        check_vma=False,
    )
```

```python
import math

import jax
import jax.numpy as jnp
from jax import lax
from jax.sharding import Mesh
from jax.sharding import PartitionSpec as P

K = 128
TILE = 128
LAYERS = 4
D_MAX = 32
HALO = LAYERS * D_MAX
CORES = 2
Y_LO = 4
TM = ("z", "ylo", "core")
ROW = ("z", "ylo")


def expand(tiles, tile):
    rows, cols = tiles.shape
    ones = tiles.astype(jnp.float32)
    return jnp.broadcast_to(ones[:, None, :, None], (rows, tile, cols, tile)).reshape(
        rows * tile, cols * tile
    )


def adam_update(factors, adam_m, adam_v, grad_f):
    m_new = 0.9 * adam_m + 0.1 * grad_f
    v_new = 0.999 * adam_v + 0.001 * grad_f * grad_f
    m_hat = m_new / (1.0 - 0.9**10)
    v_hat = v_new / (1.0 - 0.999**10)
    return (factors - 0.01 * m_hat / (jnp.sqrt(v_hat) + 1e-08), m_new, v_new)


def conv_layer(hidden, hb, past, weights, biases):
    z_val = jnp.dot(weights[0], past, preferred_element_type=jnp.float32)
    z_val = z_val + jnp.dot(weights[1], hb, preferred_element_type=jnp.float32)
    z_val = z_val + biases[:, None]
    return hidden + jax.nn.relu(z_val)


def gather_by_a2a(x, axis, count):
    copies = jnp.broadcast_to(x[None], (count,) + x.shape)
    return lax.all_to_all(copies, axis, 0, 0, tiled=True)


def on_device(y_obs, tile_mask, factors, adam_m, adam_v, basis, dilations, conv_w, conv_b):
    own_rows = factors.shape[0]
    width = basis.shape[1]
    rank_part = basis.shape[0]
    n_row = lax.axis_size(ROW)
    n_series = lax.axis_size("series")
    n_tm = n_row * CORES
    total_time = width * n_tm
    total_series = own_rows * n_tm * n_series

    fb = factors.astype(jnp.bfloat16)
    f_rows = gather_by_a2a(fb, ROW, n_row)
    core = lax.axis_index("core")
    f_other = lax.ppermute(f_rows, "core", [(0, 1), (1, 0)])

    x_parts = gather_by_a2a(basis.astype(jnp.bfloat16), "series", n_series)
    x_full = x_parts.reshape(n_series * rank_part, width)

    tiles = tile_mask.shape[0]
    mask_cols = jnp.repeat(tile_mask.astype(jnp.float32), TILE, axis=1)
    scale_f = 1.0 / math.sqrt(total_time)
    contract_time = (((1,), (1,)), ((), ()))
    y_rows = y_obs.reshape(n_row, CORES, own_rows, width)

    def half(f_half, owner):
        f2 = f_half.reshape(n_row * own_rows, K)
        y_half = lax.dynamic_index_in_dim(y_rows, owner, 1, keepdims=False)
        pred = jnp.dot(f2, x_full, preferred_element_type=jnp.float32).reshape(n_row, own_rows, width)
        gap = y_half.astype(jnp.float32) - pred
        rb = (mask_cols[:, None, :] * gap).reshape(n_row * own_rows, width).astype(jnp.bfloat16)
        part_f = -lax.dot_general(rb, x_full, contract_time, preferred_element_type=jnp.float32) * scale_f
        part_x = lax.dot_general(f2, rb, (((0,), (0,)), ((), ())), preferred_element_type=jnp.float32)
        return part_f.reshape(n_row, own_rows, K), part_x

    kept, x_mine = half(f_rows, core)
    given, x_theirs = half(f_other, 1 - core)
    by_core = kept + lax.ppermute(given.astype(jnp.bfloat16), "core", [(0, 1), (1, 0)]).astype(jnp.float32)
    by_row = lax.all_to_all(by_core.astype(jnp.bfloat16), ROW, 0, 0, tiled=True)

    partial_x = -(x_mine + x_theirs) * math.sqrt(K / total_series)
    pieces = partial_x.reshape(n_series, rank_part, width)
    by_row, sent_x = lax.optimization_barrier((by_row, pieces.astype(jnp.bfloat16)))
    arrived = lax.all_to_all(sent_x, "series", 0, 0, tiled=True)
    grad_f = by_row.astype(jnp.float32).sum(0)
    factors_new, m_new, v_new = adam_update(factors, adam_m, adam_v, grad_f)
    grad_x = arrived.astype(jnp.float32).sum(0)

    xb = x_full
    halo = lax.ppermute(xb[:, width - HALO :], TM, [(i, i + 1) for i in range(n_tm - 1)])
    first = lax.axis_index(TM) == 0
    column = lax.broadcasted_iota(jnp.int32, (1, HALO + width), 1)
    keep = jnp.logical_or(jnp.logical_not(first), column >= HALO)
    hidden = jnp.concatenate([halo, xb], axis=1).astype(jnp.float32)
    for layer in range(LAYERS):
        hb = jnp.where(keep, hidden, 0.0).astype(jnp.bfloat16)
        extended = jnp.concatenate([jnp.zeros((K, D_MAX), jnp.bfloat16), hb], axis=1)
        past = lax.dynamic_slice_in_dim(extended, D_MAX - dilations[layer], HALO + width, 1)
        hidden = conv_layer(hidden, hb, past, conv_w[layer], conv_b[layer])
    target = lax.dynamic_slice_in_dim(hidden[:, HALO:], lax.axis_index("series") * rank_part, rank_part, 0)
    basis_new = basis - 0.5 * (grad_x + (basis - target))
    return (factors_new, m_new, v_new, basis_new)


def solution(mesh):
    n_series, n_tm = mesh.devices.shape
    devices = mesh.devices.reshape(n_series, n_tm // (Y_LO * CORES), Y_LO, CORES)
    fine = Mesh(devices, ("series",) + TM)
    block = P("series", TM)
    rows = P(("series",) + TM, None)
    return jax.shard_map(
        on_device,
        mesh=fine,
        in_specs=(block, block, rows, rows, rows, block, P(), P(), P()),
        out_specs=(rows, rows, rows, block),
        check_vma=False,
    )
```

```python
import math

import jax
import jax.numpy as jnp
from jax import lax
from jax.sharding import Mesh
from jax.sharding import PartitionSpec as P

K = 128
TILE = 128
LAYERS = 4
D_MAX = 32
HALO = LAYERS * D_MAX
CORES = 2
Y_LO = 4
TM = ("z", "ylo", "core")
ROW = ("z", "ylo")


def expand(tiles, tile):
    rows, cols = tiles.shape
    ones = tiles.astype(jnp.float32)
    return jnp.broadcast_to(ones[:, None, :, None], (rows, tile, cols, tile)).reshape(
        rows * tile, cols * tile
    )


def adam_update(factors, adam_m, adam_v, grad_f):
    m_new = 0.9 * adam_m + 0.1 * grad_f
    v_new = 0.999 * adam_v + 0.001 * grad_f * grad_f
    m_hat = m_new / (1.0 - 0.9**10)
    v_hat = v_new / (1.0 - 0.999**10)
    return (factors - 0.01 * m_hat / (jnp.sqrt(v_hat) + 1e-08), m_new, v_new)


def conv_layer(hidden, hb, past, weights, biases):
    z_val = jnp.dot(weights[0], past, preferred_element_type=jnp.float32)
    z_val = z_val + jnp.dot(weights[1], hb, preferred_element_type=jnp.float32)
    z_val = z_val + biases[:, None]
    return hidden + jax.nn.relu(z_val)


def gather_by_a2a(x, axis, count):
    copies = jnp.broadcast_to(x[None], (count,) + x.shape)
    return lax.all_to_all(copies, axis, 0, 0, tiled=True)


def gather_by_doubling(x, axis, count):
    me = lax.axis_index(axis)
    held = x
    step = 1
    while step < count:
        came = lax.ppermute(held, axis, [(i, i ^ step) for i in range(count)])
        low = (me // step) % 2 == 0
        held = jnp.where(low, jnp.concatenate([held, came]), jnp.concatenate([came, held]))
        step *= 2
    return held


def on_device(y_obs, tile_mask, factors, adam_m, adam_v, basis, dilations, conv_w, conv_b):
    own_rows = factors.shape[0]
    width = basis.shape[1]
    rank_part = basis.shape[0]
    n_row = lax.axis_size(ROW)
    n_series = lax.axis_size("series")
    n_tm = n_row * CORES
    total_time = width * n_tm
    total_series = own_rows * n_tm * n_series

    fb = factors.astype(jnp.bfloat16)
    f_rows = gather_by_a2a(fb, ROW, n_row)
    core = lax.axis_index("core")
    f_other = lax.ppermute(f_rows, "core", [(0, 1), (1, 0)])

    x_full = gather_by_doubling(basis.astype(jnp.bfloat16), "series", n_series)

    tiles = tile_mask.shape[0]
    mask_cols = jnp.repeat(tile_mask.astype(jnp.float32), TILE, axis=1)
    scale_f = 1.0 / math.sqrt(total_time)
    contract_time = (((1,), (1,)), ((), ()))
    y_rows = y_obs.reshape(n_row, CORES, own_rows, width)

    def half(f_half, owner):
        f2 = f_half.reshape(n_row * own_rows, K)
        y_half = lax.dynamic_index_in_dim(y_rows, owner, 1, keepdims=False)
        pred = jnp.dot(f2, x_full, preferred_element_type=jnp.float32).reshape(n_row, own_rows, width)
        gap = y_half.astype(jnp.float32) - pred
        rb = (mask_cols[:, None, :] * gap).reshape(n_row * own_rows, width).astype(jnp.bfloat16)
        part_f = -lax.dot_general(rb, x_full, contract_time, preferred_element_type=jnp.float32) * scale_f
        part_x = lax.dot_general(f2, rb, (((0,), (0,)), ((), ())), preferred_element_type=jnp.float32)
        return part_f.reshape(n_row, own_rows, K), part_x

    kept, x_mine = half(f_rows, core)
    given, x_theirs = half(f_other, 1 - core)
    by_core = kept + lax.ppermute(given.astype(jnp.bfloat16), "core", [(0, 1), (1, 0)]).astype(jnp.float32)
    by_row = lax.all_to_all(by_core.astype(jnp.bfloat16), ROW, 0, 0, tiled=True)
    grad_f = by_row.astype(jnp.float32).sum(0)
    factors_new, m_new, v_new = adam_update(factors, adam_m, adam_v, grad_f)

    partial_x = -(x_mine + x_theirs) * math.sqrt(K / total_series)
    pieces = partial_x.reshape(n_series, rank_part, width)
    arrived = lax.all_to_all(pieces.astype(jnp.bfloat16), "series", 0, 0, tiled=True)
    grad_x = arrived.astype(jnp.float32).sum(0)

    xb = x_full
    halo = lax.ppermute(xb[:, width - HALO :], TM, [(i, i + 1) for i in range(n_tm - 1)])
    first = lax.axis_index(TM) == 0
    column = lax.broadcasted_iota(jnp.int32, (1, HALO + width), 1)
    keep = jnp.logical_or(jnp.logical_not(first), column >= HALO)
    hidden = jnp.concatenate([halo, xb], axis=1).astype(jnp.float32)
    for layer in range(LAYERS):
        hb = jnp.where(keep, hidden, 0.0).astype(jnp.bfloat16)
        extended = jnp.concatenate([jnp.zeros((K, D_MAX), jnp.bfloat16), hb], axis=1)
        past = lax.dynamic_slice_in_dim(extended, D_MAX - dilations[layer], HALO + width, 1)
        hidden = conv_layer(hidden, hb, past, conv_w[layer], conv_b[layer])
    target = lax.dynamic_slice_in_dim(hidden[:, HALO:], lax.axis_index("series") * rank_part, rank_part, 0)
    basis_new = basis - 0.5 * (grad_x + (basis - target))
    return (factors_new, m_new, v_new, basis_new)


def solution(mesh):
    n_series, n_tm = mesh.devices.shape
    devices = mesh.devices.reshape(n_series, n_tm // (Y_LO * CORES), Y_LO, CORES)
    fine = Mesh(devices, ("series",) + TM)
    block = P("series", TM)
    rows = P(("series",) + TM, None)
    return jax.shard_map(
        on_device,
        mesh=fine,
        in_specs=(block, block, rows, rows, rows, block, P(), P(), P()),
        out_specs=(rows, rows, rows, block),
        check_vma=False,
    )
```
